512 devices in a mesh: seq: 64 (over x, z, core), mp: 8 (over y).
Axes of the slice: x: 4, y: 8, z: 8, core: 2. Of those that a mesh axis runs over, the one named last changes fastest.
Arguments:
- q_new: bfloat16 [16384, 3072], P('seq', 'mp'), may hold values from -100 to 100
- k_new: bfloat16 [16384, 3072], P('seq', 'mp'), may hold values from -100 to 100
- v_new: bfloat16 [16384, 3072], P('seq', 'mp'), may hold values from -6 to 6
- q_gain: float32 [3072], P('mp'), may hold values from 0.1 to 1.9
- k_gain: float32 [3072], P('mp'), may hold values from 0.1 to 1.9
- cache_k: bfloat16 [1024, 128, 3072], P('seq', None, 'mp'), may hold values from -300 to 300
- cache_v: bfloat16 [1024, 128, 3072], P('seq', None, 'mp'), may hold values from -6 to 6
- new_count: int32 [64, 2], replicated, may hold values from 1 to 192, 256 in all within a row
- prefix_blocks: int32 [128], replicated, may hold values from 0 to 64, as said below
- block_req: int32 [1024], replicated, may hold values from 0 to 127, as said below
Outputs:
- attended: bfloat16 [16384, 3072], P('seq', 'mp')
The draws below stay inside these ranges and needn't reach their ends.
Inputs may be any that keep to these rules, and one draw needn't show every extreme that they name: Pool rows s * 16 .. (s + 1) * 16 - 1 lie on index s of seq; these blocks belong to requests of 16 different indices of seq (block_req // 2); exactly one request, the same on every index, owns one block on every index of seq (64 blocks in all). prefix_blocks[r] is the number of pool blocks b with block_req[b] = r.
All inputs are finite; a program needn't handle non-finite values.
Results may differ from the reference program's by a relative error of at most 0.015.
Values may be sent and summed in bfloat16 or wider, within the bound.
No kernel may reach another device: no remote copies, remote signals or barrier semaphores. Data moves between devices by JAX's collectives and lax.ppermute only.
A program may use at most 128 MiB of HBM per device.

```python
import math
import jax
import jax.numpy as jnp
import numpy as np
from jax import lax

HEADS = 24
HD = 128
BLOCK = 128
REQ_DEV = 2
BLK_DEV = 16
TOK_DEV = 256
HW = 3072
TOKENS = 16384
REQUESTS = 128
NBLK = 1024
N_SEQ = 64


def query_key_pair(key):
    keys = jax.random.split(jax.random.fold_in(key, 7), 3)
    width = HEADS * HD
    column_scale = 3.0 ** (jnp.arange(width, dtype=jnp.float32) / width)
    queries = jnp.clip(jax.random.normal(keys[1], (TOKENS, width), jnp.float32), -6.0, 6.0) * column_scale
    keys_out = jnp.clip(jax.random.normal(keys[2], (TOKENS, width), jnp.float32), -6.0, 6.0) * column_scale
    return (queries, keys_out)


def draw_q_new(key, part):
    return query_key_pair(key)[0].astype(jnp.bfloat16)


def draw_k_new(key, part):
    return query_key_pair(key)[1].astype(jnp.bfloat16)


def pool_map(key):
    keys = jax.random.split(jax.random.fold_in(key, 11), 5)
    hot = jax.random.randint(keys[0], (), 0, N_SEQ).astype(jnp.int32)
    hot_sub = jax.random.randint(keys[1], (), 0, REQ_DEV).astype(jnp.int32)
    row_keys = jax.random.split(keys[2], N_SEQ)
    perms = jax.vmap(lambda one: jax.random.permutation(one, N_SEQ - 1))(row_keys).astype(jnp.int32)
    others = perms[:, :BLK_DEV - 1]
    others = others + (others >= hot).astype(jnp.int32)
    dests = jnp.concatenate([jnp.zeros((N_SEQ, 1), jnp.int32) + hot, others], 1)
    shift = jax.random.randint(keys[3], (N_SEQ, 1), 0, BLK_DEV).astype(jnp.int32)
    index = (jnp.arange(BLK_DEV, dtype=jnp.int32)[None, :] + shift) % BLK_DEV
    dests = jnp.take_along_axis(dests, index, 1)
    subs = jax.random.randint(keys[4], (N_SEQ, BLK_DEV), 0, REQ_DEV).astype(jnp.int32)
    subs = jnp.where(dests == hot, hot_sub, subs)
    owners = (dests * REQ_DEV + subs).reshape(NBLK).astype(jnp.int32)
    counts = jnp.sum((owners[None, :] == jnp.arange(REQUESTS, dtype=jnp.int32)[:, None]).astype(jnp.int32), 1)
    return (owners, counts.astype(jnp.int32))


def draw_block_req(key, part):
    return pool_map(key)[0]


def draw_prefix_blocks(key, part):
    return pool_map(key)[1]


def draw_cache_k(key, part):
    keys = jax.random.split(jax.random.fold_in(key, 17), 1)
    width = HEADS * HD
    base = jnp.clip(jax.random.normal(keys[0], (NBLK, BLOCK, width), jnp.float32), -6.0, 6.0)
    return base.astype(jnp.bfloat16)


def steps_of(rng, extent, pieces, low, high):
    factor_of, own = 1.0, jax.random.fold_in(rng, 6)
    for dim, parts in pieces:
        heights = jnp.exp(jax.random.uniform(jax.random.fold_in(own, dim), (parts,), jnp.float32, low / len(pieces), high / len(pieces)))
        factor_of = factor_of * jnp.repeat(heights, extent[dim] // parts).reshape([-1 if axis == dim else 1 for axis in range(len(extent))])
    return factor_of


def profile(amount, total, bound, lean):
    loads = [(1 << 20) // math.isqrt(standing ** lean) + 1 for standing in range(2, amount + 1)]
    rest, given = total - bound - (amount - 1), [1] * (amount - 1)
    while rest > 0:
        free = [i for i in range(amount - 1) if given[i] < bound]
        pool, remaining = sum([loads[i] for i in free]), rest
        for i in free:
            addition = min(bound - given[i], max(1, remaining * loads[i] // pool), rest)
            given[i] = given[i] + addition
            rest = rest - addition
    return np.array([bound] + given)


def uneven(rng, count, total, reach, lean):
    if count == 2:
        one = jax.random.randint(rng, (), max(1, total - reach), min(reach, total - 1) + 1)
        return jnp.stack([one, total - one])
    lengths = jnp.asarray(profile(count, total, reach, lean), jnp.int32)
    couples = (count - 1) // 2
    giver, taker = lengths[1:1 + 2 * couples:2], lengths[2:2 + 2 * couples:2]
    slack = jnp.minimum(giver - 1, reach - taker)
    moved = jax.random.randint(jax.random.fold_in(rng, 1), (couples,), 0, 1 << 20) % (slack + 1)
    lengths = lengths.at[1:1 + 2 * couples:2].set(giver - moved).at[2:2 + 2 * couples:2].set(taker + moved)
    return lengths[jax.random.permutation(jax.random.fold_in(rng, 2), count)]


def scatter_about(rng, extent, deviation, limit, shards=(), held_as=jnp.bfloat16):
    drawn = deviation * jax.random.normal(rng, extent, jnp.float32)
    if shards:
        drawn = drawn * steps_of(rng, extent, shards, -0.22, 0.18)
    return jnp.clip(drawn, -limit, limit).astype(held_as)


def setup_inputs(seed: int = 0) -> dict:
    streams_of = jax.random.split(jax.random.key(seed), 11)
    q_new = draw_q_new(jax.random.fold_in(streams_of[10], 71), 0)
    k_new = draw_k_new(jax.random.fold_in(streams_of[10], 71), 0)
    v_new = scatter_about(streams_of[2], (TOKENS, HW), 1.0, 6.0, ((0, 64), (1, 8)))
    q_gain = jnp.clip(1.0 + 0.18 * jax.random.normal(streams_of[3], (HW,), jnp.float32), 0.1, 1.9)
    k_gain = jnp.clip(1.0 + 0.18 * jax.random.normal(streams_of[4], (HW,), jnp.float32), 0.1, 1.9)
    cache_k = draw_cache_k(jax.random.fold_in(streams_of[10], 71), 0)
    cache_v = scatter_about(streams_of[6], (NBLK, BLOCK, HW), 1.0, 6.0, ((0, 64), (2, 8)))
    new_count = jax.vmap(lambda own: uneven(own, REQ_DEV, TOK_DEV, 3 * TOK_DEV // 4, 1))(jax.random.split(streams_of[7], N_SEQ)).reshape((N_SEQ, REQ_DEV)).astype(jnp.int32)
    prefix_blocks = draw_prefix_blocks(jax.random.fold_in(streams_of[10], 71), 0)
    block_req = draw_block_req(jax.random.fold_in(streams_of[10], 71), 0)
    return {"q_new": q_new, "k_new": k_new, "v_new": v_new, "q_gain": q_gain, "k_gain": k_gain, "cache_k": cache_k, "cache_v": cache_v, "new_count": new_count, "prefix_blocks": prefix_blocks, "block_req": block_req}


def rotate(field, position):
    half = field.shape[-1] // 2
    freq = 500000.0 ** (-(jnp.arange(half, dtype=jnp.float32) / half))
    angle = position.astype(jnp.float32)[:, None] * freq[None, :]
    cosine = jnp.cos(angle)[:, None, :]
    sine = jnp.sin(angle)[:, None, :]
    first = field[..., :half]
    second = field[..., half:]
    return jnp.concatenate([first * cosine - second * sine, second * cosine + first * sine], -1)

def token_meta(counts, prefix, first_req, block_len, tokens_here):
    cumul = jnp.cumsum(counts, axis=1)
    starts = cumul - counts
    order = jnp.arange(tokens_here, dtype=jnp.int32)
    local = lax.optimization_barrier(jnp.sum((order[None, :, None] >= cumul[:, None, :]).astype(jnp.int32), -1))
    picker = (local[:, :, None] == jnp.arange(counts.shape[1], dtype=jnp.int32)[None, None, :]).astype(jnp.int32)
    offset = order[None, :] - lax.optimization_barrier(jnp.sum(picker * starts[:, None, :], -1))
    before = lax.optimization_barrier(jnp.sum(picker * prefix[:, None, :], -1))
    return (first_req[:, None] + local, before * block_len + offset)

def norm_rot(field, gain, position):
    values = field.astype(jnp.float32)
    squares = lax.optimization_barrier(jnp.sum(values * values, -1, keepdims=True))
    normed = values * lax.rsqrt(squares / (HEADS * HD) + 1e-06) * gain
    return rotate(normed.reshape(field.shape[0], HEADS, HD), position).astype(jnp.bfloat16)

def reference(q_new, k_new, v_new, q_gain, k_gain, cache_k, cache_v, new_count, prefix_blocks, block_req):
    first_req = jnp.arange(N_SEQ, dtype=jnp.int32) * REQ_DEV
    request, position = token_meta(new_count, prefix_blocks.reshape(N_SEQ, REQ_DEV), first_req, BLOCK, TOK_DEV)
    queries = norm_rot(q_new, q_gain, position.reshape(-1)).reshape(N_SEQ, TOK_DEV, HEADS, HD)
    keys_new = norm_rot(k_new, k_gain, position.reshape(-1)).reshape(N_SEQ, TOK_DEV, HEADS, HD)
    values_new = v_new.reshape(N_SEQ, TOK_DEV, HEADS, HD)
    scale = HD ** (-0.5)
    local_scores = jnp.einsum('nthd,nshd->nhts', queries.astype(jnp.float32), keys_new.astype(jnp.float32)) * scale
    order = jnp.arange(TOK_DEV, dtype=jnp.int32)
    allowed = (request[:, :, None] == request[:, None, :]) & (order[None, :, None] >= order[None, None, :])
    best = lax.optimization_barrier(jnp.max(jnp.where(allowed[:, None], local_scores, -1e+30), -1))

    def block_scores(owner_req, block_k):
        owner = owner_req // REQ_DEV
        here = lax.dynamic_index_in_dim(queries, owner, 0, keepdims=False)
        req_here = lax.dynamic_index_in_dim(request, owner, 0, keepdims=False)
        scores = jnp.einsum('thd,khd->htk', here.astype(jnp.float32), block_k.reshape(BLOCK, HEADS, HD).astype(jnp.float32)) * scale
        return (owner, scores, req_here == owner_req)

    def first_pass(carry, item):
        owner_req, block_k = item
        owner, scores, match = block_scores(owner_req, block_k)
        block_best = jnp.where(match[None, :], lax.optimization_barrier(jnp.max(scores, -1)), -1e+30)
        old = lax.dynamic_index_in_dim(carry, owner, 0, keepdims=False)
        return (lax.dynamic_update_index_in_dim(carry, jnp.maximum(old, block_best), owner, 0), None)
    best, _ = lax.scan(first_pass, best, (block_req, cache_k))
    weights = jnp.where(allowed[:, None], jnp.exp(local_scores - best[..., None]), 0.0)
    total = lax.optimization_barrier(jnp.sum(weights, -1))
    accum = jnp.einsum('nhts,nshd->nhtd', weights.astype(jnp.bfloat16).astype(jnp.float32), values_new.astype(jnp.float32))

    def second_pass(carry, item):
        total_all, accum_all = carry
        owner_req, block_k, block_v = item
        owner, scores, match = block_scores(owner_req, block_k)
        best_here = lax.dynamic_index_in_dim(best, owner, 0, keepdims=False)
        probs = jnp.where(match[None, :, None], jnp.exp(scores - best_here[..., None]), 0.0)
        add_total = lax.optimization_barrier(jnp.sum(probs, -1))
        add_accum = jnp.einsum('htk,khd->htd', probs.astype(jnp.bfloat16).astype(jnp.float32), block_v.reshape(BLOCK, HEADS, HD).astype(jnp.float32))
        old_total = lax.dynamic_index_in_dim(total_all, owner, 0, keepdims=False)
        old_accum = lax.dynamic_index_in_dim(accum_all, owner, 0, keepdims=False)
        total_all = lax.dynamic_update_index_in_dim(total_all, old_total + add_total, owner, 0)
        accum_all = lax.dynamic_update_index_in_dim(accum_all, old_accum + add_accum, owner, 0)
        return ((total_all, accum_all), None)
    (total, accum), _ = lax.scan(second_pass, (total, accum), (block_req, cache_k, cache_v))
    attended = (accum / total[..., None]).astype(jnp.bfloat16)
    return jnp.transpose(attended, (0, 2, 1, 3)).reshape(TOKENS, HEADS * HD)
```

```python
import jax
import jax.numpy as jnp
from jax import lax
from jax.sharding import PartitionSpec as P

HD = 128


NEGATIVE = -1e30

CAPACITIES = (24, 32, 64)


def rotate(field, position):
    half = field.shape[-1] // 2
    freq = 500000.0 ** (-(jnp.arange(half, dtype=jnp.float32) / half))
    angle = position.astype(jnp.float32)[:, None] * freq[None, :]
    cosine = jnp.cos(angle)[:, None, :]
    sine = jnp.sin(angle)[:, None, :]
    first = field[..., :half]
    second = field[..., half:]
    return jnp.concatenate([first * cosine - second * sine, second * cosine + first * sine], -1)


def token_meta(counts, prefix, first_req, block_len, tokens_here):
    cumul = jnp.cumsum(counts, axis=1)
    starts = cumul - counts
    order = jnp.arange(tokens_here, dtype=jnp.int32)
    local = jnp.sum((order[None, :, None] >= cumul[:, None, :]).astype(jnp.int32), -1)
    picker = (
        local[:, :, None] == jnp.arange(counts.shape[1], dtype=jnp.int32)[None, None, :]
    ).astype(jnp.int32)
    offset = order[None, :] - jnp.sum(picker * starts[:, None, :], -1)
    before = jnp.sum(picker * prefix[:, None, :], -1)
    return (first_req[:, None] + local, before * block_len + offset)


def partial(queries, keys_in, values_in, allowed):
    scores = jnp.einsum(
        "thd,khd->htk", queries, keys_in, preferred_element_type=jnp.float32
    ) * queries.shape[-1] ** (-0.5)
    scores = jnp.where(allowed[None], scores, NEGATIVE)
    best = jnp.max(scores, -1)
    weights = jnp.where(allowed[None], jnp.exp(scores - best[..., None]), 0.0)
    total = jnp.sum(weights, -1)
    accum = jnp.einsum(
        "htk,khd->htd", weights.astype(jnp.bfloat16), values_in, preferred_element_type=jnp.float32
    )
    return best, total, accum


def shards(
    q_new, k_new, v_new, q_gain, k_gain, cache_k, cache_v, new_count, prefix_blocks, block_req
):
    tokens_here = q_new.shape[0]
    width_here = q_new.shape[1]
    width_all = width_here * lax.axis_size("mp")
    heads_here = width_here // HD
    block_len = cache_k.shape[1]
    blocks_here = cache_k.shape[0]
    slots = lax.axis_size("seq")
    device = lax.axis_index("seq")
    per_dev = new_count.shape[1]
    rows = block_len // slots
    pool = block_req.shape[0]

    stacked = jnp.concatenate([cache_k, cache_v], -1).reshape(
        blocks_here, slots, rows, 2 * width_here
    )
    spread = lax.all_to_all(stacked, "seq", split_axis=1, concat_axis=1, tiled=True)
    pieces = spread.reshape(blocks_here * slots, rows, 2 * width_here)

    query_f = q_new.astype(jnp.float32)
    key_f = k_new.astype(jnp.float32)
    square_q, square_k = lax.psum(
        (jnp.sum(query_f * query_f, -1), jnp.sum(key_f * key_f, -1)), "mp"
    )
    first_all = jnp.arange(slots, dtype=jnp.int32) * per_dev
    req_all, pos_all = token_meta(
        new_count, prefix_blocks.reshape(slots, per_dev), first_all, block_len, tokens_here
    )
    query_req = lax.dynamic_index_in_dim(req_all, device, 0, keepdims=False)
    position = lax.dynamic_index_in_dim(pos_all, device, 0, keepdims=False)
    normed_q = query_f * lax.rsqrt(square_q / width_all + 1e-06)[:, None] * q_gain
    normed_k = key_f * lax.rsqrt(square_k / width_all + 1e-06)[:, None] * k_gain
    queries = rotate(normed_q.reshape(tokens_here, heads_here, HD), position).astype(jnp.bfloat16)
    keys_here = rotate(normed_k.reshape(tokens_here, heads_here, HD), position).astype(jnp.bfloat16)
    values_here = v_new.reshape(tokens_here, heads_here, HD)

    order = jnp.arange(tokens_here, dtype=jnp.int32)
    causal = (query_req[:, None] == query_req[None, :]) & (order[:, None] >= order[None, :])
    own = partial(queries, keys_here, values_here, causal)

    hot = jnp.argmax(prefix_blocks).astype(jnp.int32)
    hot_dev = hot // per_dev
    hot_queries = lax.psum(
        jnp.where(device == hot_dev, queries, jnp.zeros((), jnp.bfloat16)), "seq"
    )
    owner_here = lax.dynamic_index_in_dim(
        block_req.reshape(slots, blocks_here), device, 0, keepdims=False
    )
    hot_slot = jnp.argmax(owner_here == hot).astype(jnp.int32)
    hot_keys = lax.dynamic_index_in_dim(cache_k, hot_slot, 0, keepdims=False)
    hot_values = lax.dynamic_index_in_dim(cache_v, hot_slot, 0, keepdims=False)
    hot_scores = jnp.einsum(
        "thd,khd->htk",
        hot_queries,
        hot_keys.reshape(block_len, heads_here, HD),
        preferred_element_type=jnp.float32,
    ) * HD ** (-0.5)
    hot_best = lax.pmax(jnp.max(hot_scores, -1), "seq")
    hot_weights = jnp.exp(hot_scores - hot_best[..., None])
    hot_total, hot_accum = lax.psum(
        (
            jnp.sum(hot_weights, -1),
            jnp.einsum(
                "htk,khd->htd",
                hot_weights.astype(jnp.bfloat16),
                hot_values.reshape(block_len, heads_here, HD),
                preferred_element_type=jnp.float32,
            ),
        ),
        "seq",
    )

    dest = block_req // per_dev
    onehot = (dest[:, None] == jnp.arange(slots, dtype=jnp.int32)[None, :]) & (
        block_req != hot
    )[:, None]
    rank = jnp.sum(jnp.where(onehot, jnp.cumsum(onehot.astype(jnp.int32), 0) - 1, 0), 1)
    counts = jnp.sum(onehot.astype(jnp.int32), 0)
    widest = CAPACITIES[-1]
    match = onehot.T[:, None, :] & (
        rank[None, None, :] == jnp.arange(widest, dtype=jnp.int32)[None, :, None]
    )
    ids = jnp.arange(pool, dtype=jnp.int32)
    table = jnp.sum(jnp.where(match, ids[None, None, :], 0), -1)
    present = jnp.any(match, -1)
    tags = jnp.where(present, block_req[table], -1)
    mine_tags = lax.dynamic_index_in_dim(tags, device, 0, keepdims=False)
    source = (table % blocks_here) * slots + table // blocks_here

    def cached(capacity):
        def run(pieces, source, present, mine_tags, queries, query_req):
            pick = source[:, :capacity].reshape(-1)
            send = jnp.where(
                present[:, :capacity, None, None],
                jnp.take(pieces, pick, axis=0).reshape(slots, capacity, rows, 2 * width_here),
                jnp.zeros((), jnp.bfloat16),
            )
            got = lax.all_to_all(send, "seq", split_axis=0, concat_axis=0, tiled=True)
            got = got.reshape(slots * capacity * rows, 2, heads_here, HD)
            key_req = jnp.broadcast_to(
                mine_tags[None, :capacity, None], (slots, capacity, rows)
            ).reshape(-1)
            allowed = query_req[:, None] == key_req[None, :]
            return partial(queries, got[:, 0], got[:, 1], allowed)

        return run

    level = jnp.sum((jnp.max(counts) > jnp.array(CAPACITIES[:-1], jnp.int32)).astype(jnp.int32))
    far = lax.switch(
        level,
        [cached(c) for c in CAPACITIES],
        pieces,
        source,
        present,
        mine_tags,
        queries,
        query_req,
    )

    hot_here = query_req == hot
    hot_best = jnp.where(hot_here[None, :], hot_best, NEGATIVE)
    hot_total = jnp.where(hot_here[None, :], hot_total, 0.0)
    hot_accum = jnp.where(hot_here[None, :, None], hot_accum, 0.0)
    parts = (own, far, (hot_best, hot_total, hot_accum))
    best = jnp.maximum(jnp.maximum(own[0], far[0]), hot_best)
    total = 0.0
    accum = 0.0
    for part_best, part_total, part_accum in parts:
        factor = jnp.exp(part_best - best)
        total = total + part_total * factor
        accum = accum + part_accum * factor[..., None]
    result = (accum / total[..., None]).astype(jnp.bfloat16)
    return jnp.transpose(result, (1, 0, 2)).reshape(tokens_here, heads_here * HD)


def solution(mesh):
    return jax.shard_map(
        shards,
        mesh=mesh,
        in_specs=(
            P("seq", "mp"),
            P("seq", "mp"),
            P("seq", "mp"),
            P("mp"),
            P("mp"),
            P("seq", None, "mp"),
            P("seq", None, "mp"),
            P(),
            P(),
            P(),
        ),
        out_specs=P("seq", "mp"),
        check_vma=False,
    )
```

```python
import jax
import jax.numpy as jnp
from jax import lax
from jax.sharding import PartitionSpec as P

HD = 128


NEGATIVE = -1e30

CAPACITIES = (24, 32, 64)


def rotate(field, position):
    half = field.shape[-1] // 2
    freq = 500000.0 ** (-(jnp.arange(half, dtype=jnp.float32) / half))
    angle = position.astype(jnp.float32)[:, None] * freq[None, :]
    cosine = jnp.cos(angle)[:, None, :]
    sine = jnp.sin(angle)[:, None, :]
    first = field[..., :half]
    second = field[..., half:]
    return jnp.concatenate([first * cosine - second * sine, second * cosine + first * sine], -1)


def token_meta(counts, prefix, first_req, block_len, tokens_here):
    cumul = jnp.cumsum(counts, axis=1)
    starts = cumul - counts
    order = jnp.arange(tokens_here, dtype=jnp.int32)
    local = jnp.sum((order[None, :, None] >= cumul[:, None, :]).astype(jnp.int32), -1)
    picker = (
        local[:, :, None] == jnp.arange(counts.shape[1], dtype=jnp.int32)[None, None, :]
    ).astype(jnp.int32)
    offset = order[None, :] - jnp.sum(picker * starts[:, None, :], -1)
    before = jnp.sum(picker * prefix[:, None, :], -1)
    return (first_req[:, None] + local, before * block_len + offset)


def partial(queries, keys_in, values_in, allowed):
    scores = jnp.einsum(
        "thd,khd->htk", queries, keys_in, preferred_element_type=jnp.float32
    ) * queries.shape[-1] ** (-0.5)
    scores = jnp.where(allowed[None], scores, NEGATIVE)
    best = jnp.max(scores, -1)
    weights = jnp.where(allowed[None], jnp.exp(scores - best[..., None]), 0.0)
    total = jnp.sum(weights, -1)
    accum = jnp.einsum(
        "htk,khd->htd", weights.astype(jnp.bfloat16), values_in, preferred_element_type=jnp.float32
    )
    return best, total, accum


def shards(
    q_new, k_new, v_new, q_gain, k_gain, cache_k, cache_v, new_count, prefix_blocks, block_req
):
    tokens_here = q_new.shape[0]
    width_here = q_new.shape[1]
    width_all = width_here * lax.axis_size("mp")
    heads_here = width_here // HD
    block_len = cache_k.shape[1]
    blocks_here = cache_k.shape[0]
    slots = lax.axis_size("seq")
    device = lax.axis_index("seq")
    per_dev = new_count.shape[1]
    rows = block_len // slots
    pool = block_req.shape[0]

    stacked = jnp.concatenate([cache_k, cache_v], -1).reshape(
        blocks_here, slots, rows, 2 * width_here
    )
    spread = lax.all_to_all(stacked, "seq", split_axis=1, concat_axis=1, tiled=True)
    pieces = spread.reshape(blocks_here * slots, rows, 2 * width_here)

    query_f = q_new.astype(jnp.float32)
    key_f = k_new.astype(jnp.float32)
    square_q, square_k = lax.psum(
        (jnp.sum(query_f * query_f, -1), jnp.sum(key_f * key_f, -1)), "mp"
    )
    first_all = jnp.arange(slots, dtype=jnp.int32) * per_dev
    req_all, pos_all = token_meta(
        new_count, prefix_blocks.reshape(slots, per_dev), first_all, block_len, tokens_here
    )
    query_req = lax.dynamic_index_in_dim(req_all, device, 0, keepdims=False)
    position = lax.dynamic_index_in_dim(pos_all, device, 0, keepdims=False)
    normed_q = query_f * lax.rsqrt(square_q / width_all + 1e-06)[:, None] * q_gain
    normed_k = key_f * lax.rsqrt(square_k / width_all + 1e-06)[:, None] * k_gain
    queries = rotate(normed_q.reshape(tokens_here, heads_here, HD), position).astype(jnp.bfloat16)
    keys_here = rotate(normed_k.reshape(tokens_here, heads_here, HD), position).astype(jnp.bfloat16)
    values_here = v_new.reshape(tokens_here, heads_here, HD)

    order = jnp.arange(tokens_here, dtype=jnp.int32)
    causal = (query_req[:, None] == query_req[None, :]) & (order[:, None] >= order[None, :])
    own = partial(queries, keys_here, values_here, causal)

    hot = jnp.argmax(prefix_blocks).astype(jnp.int32)
    hot_dev = hot // per_dev
    piece = tokens_here // slots
    spread_q = lax.all_to_all(
        queries.reshape(slots, piece, heads_here, HD), "seq", split_axis=0, concat_axis=0, tiled=True
    )
    mine_q = lax.dynamic_index_in_dim(spread_q, hot_dev, 0, keepdims=False)
    hot_queries = lax.all_to_all(
        jnp.broadcast_to(mine_q[None], (slots, piece, heads_here, HD)),
        "seq",
        split_axis=0,
        concat_axis=0,
        tiled=True,
    ).reshape(tokens_here, heads_here, HD)
    owner_here = lax.dynamic_index_in_dim(
        block_req.reshape(slots, blocks_here), device, 0, keepdims=False
    )
    hot_slot = jnp.argmax(owner_here == hot).astype(jnp.int32)
    hot_keys = lax.dynamic_index_in_dim(cache_k, hot_slot, 0, keepdims=False)
    hot_values = lax.dynamic_index_in_dim(cache_v, hot_slot, 0, keepdims=False)
    every = jnp.ones((tokens_here, block_len), bool)
    hot_part = partial(
        hot_queries,
        hot_keys.reshape(block_len, heads_here, HD),
        hot_values.reshape(block_len, heads_here, HD),
        every,
    )
    packed = jnp.concatenate(
        [hot_part[2], hot_part[0][..., None], hot_part[1][..., None]], -1
    ).reshape(heads_here, slots, piece, HD + 2)
    gathered = lax.all_to_all(
        jnp.transpose(packed, (1, 0, 2, 3)), "seq", split_axis=0, concat_axis=0, tiled=True
    )
    piece_best = jnp.max(gathered[..., HD], 0)
    piece_factor = jnp.exp(gathered[..., HD] - piece_best[None])
    merged = jnp.concatenate(
        [
            jnp.sum(gathered[..., :HD] * piece_factor[..., None], 0),
            piece_best[..., None],
            jnp.sum(gathered[..., HD + 1] * piece_factor, 0)[..., None],
        ],
        -1,
    )
    returned = lax.all_to_all(
        jnp.broadcast_to(merged[None], (slots,) + merged.shape),
        "seq",
        split_axis=0,
        concat_axis=0,
        tiled=True,
    )
    returned = jnp.transpose(returned, (1, 0, 2, 3)).reshape(heads_here, tokens_here, HD + 2)
    hot_accum = returned[..., :HD]
    hot_best = returned[..., HD]
    hot_total = returned[..., HD + 1]

    targets = jnp.arange(slots, dtype=jnp.int32)
    owner_table = block_req.reshape(slots, blocks_here)
    usable = owner_table != hot
    hit = ((owner_table // per_dev)[:, :, None] == targets[None, None, :]) & usable[:, :, None]
    has = jnp.any(hit, 1)
    slot_of = jnp.sum(jnp.where(hit, jnp.arange(blocks_here, dtype=jnp.int32)[None, :, None], 0), 1)
    req_of = jnp.sum(jnp.where(hit, owner_table[:, :, None], 0), 1)
    lower = (targets[:, None] > targets[None, :]).astype(jnp.bfloat16)
    rank = jnp.einsum(
        "st,td->sd", lower, has.astype(jnp.bfloat16), preferred_element_type=jnp.float32
    ).astype(jnp.int32)
    counts = jnp.sum(has.astype(jnp.int32), 0)
    widest = CAPACITIES[-1]
    match = has[None] & (rank[None] == jnp.arange(widest, dtype=jnp.int32)[:, None, None])
    sources = targets[None, :, None]
    source = jnp.transpose(
        jnp.sum(jnp.where(match, slot_of[None] * slots + sources, 0), 1)
    )
    present = jnp.transpose(jnp.any(match, 1))
    tags = jnp.transpose(jnp.where(jnp.any(match, 1), jnp.sum(jnp.where(match, req_of[None], 0), 1), -1))
    mine_tags = lax.dynamic_index_in_dim(tags, device, 0, keepdims=False)

    def cached(capacity):
        def run(pieces, source, present, mine_tags, queries, query_req):
            pick = source[:, :capacity].reshape(-1)
            send = jnp.where(
                present[:, :capacity, None, None],
                jnp.take(pieces, pick, axis=0).reshape(slots, capacity, rows, 2 * width_here),
                jnp.zeros((), jnp.bfloat16),
            )
            got = lax.all_to_all(send, "seq", split_axis=0, concat_axis=0, tiled=True)
            got = got.reshape(slots * capacity * rows, 2, heads_here, HD)
            key_req = jnp.broadcast_to(
                mine_tags[None, :capacity, None], (slots, capacity, rows)
            ).reshape(-1)
            allowed = query_req[:, None] == key_req[None, :]
            return partial(queries, got[:, 0], got[:, 1], allowed)

        return run

    level = jnp.sum((jnp.max(counts) > jnp.array(CAPACITIES[:-1], jnp.int32)).astype(jnp.int32))
    far = lax.switch(
        level,
        [cached(c) for c in CAPACITIES],
        pieces,
        source,
        present,
        mine_tags,
        queries,
        query_req,
    )

    hot_here = query_req == hot
    hot_best = jnp.where(hot_here[None, :], hot_best, NEGATIVE)
    hot_total = jnp.where(hot_here[None, :], hot_total, 0.0)
    hot_accum = jnp.where(hot_here[None, :, None], hot_accum, 0.0)
    parts = (own, far, (hot_best, hot_total, hot_accum))
    best = jnp.maximum(jnp.maximum(own[0], far[0]), hot_best)
    total = 0.0
    accum = 0.0
    for part_best, part_total, part_accum in parts:
        factor = jnp.exp(part_best - best)
        total = total + part_total * factor
        accum = accum + part_accum * factor[..., None]
    result = (accum / total[..., None]).astype(jnp.bfloat16)
    return jnp.transpose(result, (1, 0, 2)).reshape(tokens_here, heads_here * HD)


def solution(mesh):
    return jax.shard_map(
        shards,
        mesh=mesh,
        in_specs=(
            P("seq", "mp"),
            P("seq", "mp"),
            P("seq", "mp"),
            P("mp"),
            P("mp"),
            P("seq", None, "mp"),
            P("seq", None, "mp"),
            P(),
            P(),
            P(),
        ),
        out_specs=P("seq", "mp"),
        check_vma=False,
    )
```

```python
import jax
import jax.numpy as jnp
from jax import lax
from jax.sharding import PartitionSpec as P

HD = 128


NEGATIVE = -1e30

CAPACITIES = (24, 32, 64)


def rotate(field, position):
    half = field.shape[-1] // 2
    freq = 500000.0 ** (-(jnp.arange(half, dtype=jnp.float32) / half))
    angle = position.astype(jnp.float32)[:, None] * freq[None, :]
    cosine = jnp.cos(angle)[:, None, :]
    sine = jnp.sin(angle)[:, None, :]
    first = field[..., :half]
    second = field[..., half:]
    return jnp.concatenate([first * cosine - second * sine, second * cosine + first * sine], -1)


def token_meta(counts, prefix, first_req, block_len, tokens_here):
    cumul = jnp.cumsum(counts, axis=1)
    starts = cumul - counts
    order = jnp.arange(tokens_here, dtype=jnp.int32)
    local = jnp.sum((order[None, :, None] >= cumul[:, None, :]).astype(jnp.int32), -1)
    picker = (
        local[:, :, None] == jnp.arange(counts.shape[1], dtype=jnp.int32)[None, None, :]
    ).astype(jnp.int32)
    offset = order[None, :] - jnp.sum(picker * starts[:, None, :], -1)
    before = jnp.sum(picker * prefix[:, None, :], -1)
    return (first_req[:, None] + local, before * block_len + offset)


def partial(queries, keys_in, values_in, allowed):
    scores = jnp.einsum(
        "thd,khd->htk", queries, keys_in, preferred_element_type=jnp.float32
    ) * queries.shape[-1] ** (-0.5)
    scores = jnp.where(allowed[None], scores, NEGATIVE)
    best = jnp.max(scores, -1)
    weights = jnp.where(allowed[None], jnp.exp(scores - best[..., None]), 0.0)
    total = jnp.sum(weights, -1)
    accum = jnp.einsum(
        "htk,khd->htd", weights.astype(jnp.bfloat16), values_in, preferred_element_type=jnp.float32
    )
    return best, total, accum


def shards(
    q_new, k_new, v_new, q_gain, k_gain, cache_k, cache_v, new_count, prefix_blocks, block_req
):
    tokens_here = q_new.shape[0]
    width_here = q_new.shape[1]
    width_all = width_here * lax.axis_size("mp")
    heads_here = width_here // HD
    block_len = cache_k.shape[1]
    blocks_here = cache_k.shape[0]
    slots = lax.axis_size("seq")
    device = lax.axis_index("seq")
    per_dev = new_count.shape[1]
    rows = block_len // slots
    pool = block_req.shape[0]

    query_f = q_new.astype(jnp.float32)
    key_f = k_new.astype(jnp.float32)
    square_q, square_k = lax.psum(
        (jnp.sum(query_f * query_f, -1), jnp.sum(key_f * key_f, -1)), "mp"
    )
    first_all = jnp.arange(slots, dtype=jnp.int32) * per_dev
    req_all, pos_all = token_meta(
        new_count, prefix_blocks.reshape(slots, per_dev), first_all, block_len, tokens_here
    )
    query_req = lax.dynamic_index_in_dim(req_all, device, 0, keepdims=False)
    position = lax.dynamic_index_in_dim(pos_all, device, 0, keepdims=False)
    normed_q = query_f * lax.rsqrt(square_q / width_all + 1e-06)[:, None] * q_gain
    normed_k = key_f * lax.rsqrt(square_k / width_all + 1e-06)[:, None] * k_gain
    queries = rotate(normed_q.reshape(tokens_here, heads_here, HD), position).astype(jnp.bfloat16)
    keys_here = rotate(normed_k.reshape(tokens_here, heads_here, HD), position).astype(jnp.bfloat16)
    values_here = v_new.reshape(tokens_here, heads_here, HD)

    piece = tokens_here // slots
    piece_len = piece * width_here
    chunk = blocks_here * rows * 2 * width_here
    stacked = jnp.concatenate([cache_k, cache_v], -1).reshape(
        blocks_here, slots, chunk // blocks_here
    )
    outgoing = jnp.concatenate(
        [
            jnp.transpose(stacked, (1, 0, 2)).reshape(slots, chunk),
            queries.reshape(slots, piece_len),
        ],
        1,
    )
    incoming = lax.all_to_all(outgoing, "seq", split_axis=0, concat_axis=0, tiled=True)
    pieces = incoming[:, :chunk].reshape(pool, rows * 2 * width_here)
    query_pieces = incoming[:, chunk:]

    order = jnp.arange(tokens_here, dtype=jnp.int32)
    causal = (query_req[:, None] == query_req[None, :]) & (order[:, None] >= order[None, :])
    own = partial(queries, keys_here, values_here, causal)

    hot = jnp.argmax(prefix_blocks).astype(jnp.int32)
    hot_dev = hot // per_dev
    mine_q = lax.dynamic_index_in_dim(query_pieces, hot_dev, 0, keepdims=False)
    owner_here = lax.dynamic_index_in_dim(
        block_req.reshape(slots, blocks_here), device, 0, keepdims=False
    )
    hot_slot = jnp.argmax(owner_here == hot).astype(jnp.int32)
    hot_keys = lax.dynamic_index_in_dim(cache_k, hot_slot, 0, keepdims=False)
    hot_values = lax.dynamic_index_in_dim(cache_v, hot_slot, 0, keepdims=False)

    targets = jnp.arange(slots, dtype=jnp.int32)
    owner_table = block_req.reshape(slots, blocks_here)
    usable = owner_table != hot
    hit = ((owner_table // per_dev)[:, :, None] == targets[None, None, :]) & usable[:, :, None]
    has = jnp.any(hit, 1)
    slot_of = jnp.sum(jnp.where(hit, jnp.arange(blocks_here, dtype=jnp.int32)[None, :, None], 0), 1)
    req_of = jnp.sum(jnp.where(hit, owner_table[:, :, None], 0), 1)
    lower = (targets[:, None] > targets[None, :]).astype(jnp.bfloat16)
    rank = jnp.einsum(
        "st,td->sd", lower, has.astype(jnp.bfloat16), preferred_element_type=jnp.float32
    ).astype(jnp.int32)
    counts = jnp.sum(has.astype(jnp.int32), 0)
    widest = CAPACITIES[-1]
    match = has[None] & (rank[None] == jnp.arange(widest, dtype=jnp.int32)[:, None, None])
    sources = targets[None, :, None]
    source = jnp.transpose(
        jnp.sum(jnp.where(match, sources * blocks_here + slot_of[None], 0), 1)
    )
    tags = jnp.transpose(
        jnp.where(jnp.any(match, 1), jnp.sum(jnp.where(match, req_of[None], 0), 1), -1)
    )
    mine_tags = lax.dynamic_index_in_dim(tags, device, 0, keepdims=False)
    hot_here = query_req == hot

    def cached(capacity):
        def run(pieces, source, mine_tags, mine_q, queries, query_req, hot_keys, hot_values):
            send = jnp.take(pieces, source[:, :capacity].reshape(-1), axis=0).reshape(
                slots, capacity * rows * 2 * width_here
            )
            send = jnp.concatenate(
                [send, jnp.broadcast_to(mine_q[None], (slots, piece_len))], 1
            )
            got = lax.all_to_all(send, "seq", split_axis=0, concat_axis=0, tiled=True)
            hot_queries = got[:, capacity * rows * 2 * width_here :].reshape(
                tokens_here, heads_here, HD
            )

            every = jnp.ones((tokens_here, block_len), bool)
            hot_part = partial(
                hot_queries,
                hot_keys.reshape(block_len, heads_here, HD),
                hot_values.reshape(block_len, heads_here, HD),
                every,
            )
            packed = jnp.concatenate(
                [hot_part[2], hot_part[0][..., None], hot_part[1][..., None]], -1
            ).reshape(heads_here, slots, piece, HD + 2)
            gathered = lax.all_to_all(
                jnp.transpose(packed, (1, 0, 2, 3)), "seq", split_axis=0, concat_axis=0, tiled=True
            )
            piece_best = jnp.max(gathered[..., HD], 0)
            piece_factor = jnp.exp(gathered[..., HD] - piece_best[None])
            merged = jnp.concatenate(
                [
                    jnp.sum(gathered[..., :HD] * piece_factor[..., None], 0),
                    piece_best[..., None],
                    jnp.sum(gathered[..., HD + 1] * piece_factor, 0)[..., None],
                ],
                -1,
            )
            returned = lax.all_to_all(
                jnp.broadcast_to(merged[None], (slots,) + merged.shape),
                "seq",
                split_axis=0,
                concat_axis=0,
                tiled=True,
            )
            returned = jnp.transpose(returned, (1, 0, 2, 3)).reshape(
                heads_here, tokens_here, HD + 2
            )

            blocks_in = got[:, : capacity * rows * 2 * width_here].reshape(
                slots * capacity * rows, 2, heads_here, HD
            )
            key_req = jnp.broadcast_to(
                mine_tags[None, :capacity, None], (slots, capacity, rows)
            ).reshape(-1)
            allowed = query_req[:, None] == key_req[None, :]
            far = partial(queries, blocks_in[:, 0], blocks_in[:, 1], allowed)
            return far, (returned[..., HD], returned[..., HD + 1], returned[..., :HD])

        return run

    level = jnp.sum((jnp.max(counts) > jnp.array(CAPACITIES[:-1], jnp.int32)).astype(jnp.int32))
    far, (hot_best, hot_total, hot_accum) = lax.switch(
        level,
        [cached(c) for c in CAPACITIES],
        pieces,
        source,
        mine_tags,
        mine_q,
        queries,
        query_req,
        hot_keys,
        hot_values,
    )

    hot_best = jnp.where(hot_here[None, :], hot_best, NEGATIVE)
    hot_total = jnp.where(hot_here[None, :], hot_total, 0.0)
    hot_accum = jnp.where(hot_here[None, :, None], hot_accum, 0.0)
    parts = (own, far, (hot_best, hot_total, hot_accum))
    best = jnp.maximum(jnp.maximum(own[0], far[0]), hot_best)
    total = 0.0
    accum = 0.0
    for part_best, part_total, part_accum in parts:
        factor = jnp.exp(part_best - best)
        total = total + part_total * factor
        accum = accum + part_accum * factor[..., None]
    result = (accum / total[..., None]).astype(jnp.bfloat16)
    return jnp.transpose(result, (1, 0, 2)).reshape(tokens_here, heads_here * HD)


def solution(mesh):
    return jax.shard_map(
        shards,
        mesh=mesh,
        in_specs=(
            P("seq", "mp"),
            P("seq", "mp"),
            P("seq", "mp"),
            P("mp"),
            P("mp"),
            P("seq", None, "mp"),
            P("seq", None, "mp"),
            P(),
            P(),
            P(),
        ),
        out_specs=P("seq", "mp"),
        check_vma=False,
    )
```

```python
import jax
import jax.numpy as jnp
from jax import lax
from jax.sharding import PartitionSpec as P

HD = 128


NEGATIVE = -1e30


def rotate(field, position):
    half = field.shape[-1] // 2
    freq = 500000.0 ** (-(jnp.arange(half, dtype=jnp.float32) / half))
    angle = position.astype(jnp.float32)[:, None] * freq[None, :]
    cosine = jnp.cos(angle)[:, None, :]
    sine = jnp.sin(angle)[:, None, :]
    first = field[..., :half]
    second = field[..., half:]
    return jnp.concatenate([first * cosine - second * sine, second * cosine + first * sine], -1)


def token_meta(counts, prefix, first_req, block_len, tokens_here):
    cumul = jnp.cumsum(counts, axis=1)
    starts = cumul - counts
    order = jnp.arange(tokens_here, dtype=jnp.int32)
    local = jnp.sum((order[None, :, None] >= cumul[:, None, :]).astype(jnp.int32), -1)
    picker = (
        local[:, :, None] == jnp.arange(counts.shape[1], dtype=jnp.int32)[None, None, :]
    ).astype(jnp.int32)
    offset = order[None, :] - jnp.sum(picker * starts[:, None, :], -1)
    before = jnp.sum(picker * prefix[:, None, :], -1)
    return (first_req[:, None] + local, before * block_len + offset)


def head_partial(queries, keys_in, values_in, allowed):
    scores = jnp.einsum(
        "td,kd->tk", queries, keys_in, preferred_element_type=jnp.float32
    ) * queries.shape[-1] ** (-0.5)
    scores = jnp.where(allowed, scores, NEGATIVE)
    best = jnp.max(scores, -1)
    weights = jnp.where(allowed, jnp.exp(scores - best[:, None]), 0.0)
    total = jnp.sum(weights, -1)
    return best, total, weights.astype(jnp.bfloat16)


def shards(
    q_new, k_new, v_new, q_gain, k_gain, cache_k, cache_v, new_count, prefix_blocks, block_req
):
    tokens_here = q_new.shape[0]
    width_all = q_new.shape[1] * lax.axis_size("mp")
    heads_here = q_new.shape[1] // HD
    block_len = cache_k.shape[1]
    blocks_here = cache_k.shape[0]
    slots = lax.axis_size("seq")
    device = lax.axis_index("seq")
    per_dev = new_count.shape[1]

    owner_table = block_req.reshape(slots, blocks_here)
    dest_table = owner_table // per_dev
    targets = jnp.arange(slots, dtype=jnp.int32)
    mine = lax.dynamic_index_in_dim(dest_table, device, 0, keepdims=False)
    hit = mine[None, :] == targets[:, None]
    arrive = dest_table == device
    picks = jnp.sum(jnp.where(hit, jnp.arange(blocks_here, dtype=jnp.int32)[None, :], 0), 1)
    got_keys = lax.all_to_all(
        jnp.take(cache_k, picks, axis=0), "seq", split_axis=0, concat_axis=0, tiled=True
    )
    got_values = lax.all_to_all(
        jnp.take(cache_v, picks, axis=0), "seq", split_axis=0, concat_axis=0, tiled=True
    )
    slot_req = jnp.where(jnp.any(arrive, 1), jnp.sum(jnp.where(arrive, owner_table, 0), 1), -1)
    key_req = jnp.repeat(slot_req, block_len)
    keys_all = got_keys.reshape(slots * block_len, -1)
    values_all = got_values.reshape(slots * block_len, -1)

    query_f = q_new.astype(jnp.float32)
    key_f = k_new.astype(jnp.float32)
    square_q, square_k = lax.psum(
        (jnp.sum(query_f * query_f, -1), jnp.sum(key_f * key_f, -1)), "mp"
    )
    first_all = jnp.arange(slots, dtype=jnp.int32) * per_dev
    req_all, pos_all = token_meta(
        new_count, prefix_blocks.reshape(slots, per_dev), first_all, block_len, tokens_here
    )
    query_req = lax.dynamic_index_in_dim(req_all, device, 0, keepdims=False)
    position = lax.dynamic_index_in_dim(pos_all, device, 0, keepdims=False)
    normed_q = query_f * lax.rsqrt(square_q / width_all + 1e-06)[:, None] * q_gain
    normed_k = key_f * lax.rsqrt(square_k / width_all + 1e-06)[:, None] * k_gain
    queries = rotate(normed_q.reshape(tokens_here, heads_here, HD), position).astype(jnp.bfloat16)
    keys_here = rotate(normed_k.reshape(tokens_here, heads_here, HD), position).astype(jnp.bfloat16)
    order = jnp.arange(tokens_here, dtype=jnp.int32)
    causal = (query_req[:, None] == query_req[None, :]) & (order[:, None] >= order[None, :])
    seen = query_req[:, None] == key_req[None, :]

    heads = []
    for head in range(heads_here):
        cols = slice(head * HD, (head + 1) * HD)
        query_h = queries[:, head]
        best_n, total_n, weights_n = head_partial(query_h, keys_here[:, head], None, causal)
        best_c, total_c, weights_c = head_partial(query_h, keys_all[:, cols], None, seen)
        best = jnp.maximum(best_n, best_c)
        factor_n = jnp.exp(best_n - best)
        factor_c = jnp.exp(best_c - best)
        total = total_n * factor_n + total_c * factor_c
        accum = jnp.einsum(
            "tk,kd->td", weights_n, v_new[:, cols], preferred_element_type=jnp.float32
        ) * factor_n[:, None] + jnp.einsum(
            "tk,kd->td", weights_c, values_all[:, cols], preferred_element_type=jnp.float32
        ) * factor_c[:, None]
        heads.append((accum / total[:, None]).astype(jnp.bfloat16))
    return jnp.concatenate(heads, -1)


def solution(mesh):
    return jax.shard_map(
        shards,
        mesh=mesh,
        in_specs=(
            P("seq", "mp"),
            P("seq", "mp"),
            P("seq", "mp"),
            P("mp"),
            P("mp"),
            P("seq", None, "mp"),
            P("seq", None, "mp"),
            P(),
            P(),
            P(),
        ),
        out_specs=P("seq", "mp"),
        check_vma=False,
    )
```

```python
import jax
import jax.numpy as jnp
from jax import lax
from jax.sharding import PartitionSpec as P

HD = 128


NEGATIVE = -1e30


def rotate(field, position):
    half = field.shape[-1] // 2
    freq = 500000.0 ** (-(jnp.arange(half, dtype=jnp.float32) / half))
    angle = position.astype(jnp.float32)[:, None] * freq[None, :]
    cosine = jnp.cos(angle)[:, None, :]
    sine = jnp.sin(angle)[:, None, :]
    first = field[..., :half]
    second = field[..., half:]
    return jnp.concatenate([first * cosine - second * sine, second * cosine + first * sine], -1)


def token_meta(counts, prefix, first_req, block_len, tokens_here):
    cumul = jnp.cumsum(counts, axis=1)
    starts = cumul - counts
    order = jnp.arange(tokens_here, dtype=jnp.int32)
    local = jnp.sum((order[None, :, None] >= cumul[:, None, :]).astype(jnp.int32), -1)
    picker = (
        local[:, :, None] == jnp.arange(counts.shape[1], dtype=jnp.int32)[None, None, :]
    ).astype(jnp.int32)
    offset = order[None, :] - jnp.sum(picker * starts[:, None, :], -1)
    before = jnp.sum(picker * prefix[:, None, :], -1)
    return (first_req[:, None] + local, before * block_len + offset)


def head_partial(queries, keys_in, values_in, allowed):
    scores = jnp.einsum(
        "td,kd->tk", queries, keys_in, preferred_element_type=jnp.float32
    ) * queries.shape[-1] ** (-0.5)
    scores = jnp.where(allowed, scores, NEGATIVE)
    best = jnp.max(scores, -1)
    weights = jnp.where(allowed, jnp.exp(scores - best[:, None]), 0.0)
    total = jnp.sum(weights, -1)
    return best, total, weights.astype(jnp.bfloat16)


def shards(
    q_new, k_new, v_new, q_gain, k_gain, cache_k, cache_v, new_count, prefix_blocks, block_req
):
    tokens_here = q_new.shape[0]
    width_all = q_new.shape[1] * lax.axis_size("mp")
    heads_here = q_new.shape[1] // HD
    block_len = cache_k.shape[1]
    blocks_here = cache_k.shape[0]
    slots = lax.axis_size("seq")
    device = lax.axis_index("seq")
    per_dev = new_count.shape[1]

    owner_table = block_req.reshape(slots, blocks_here)
    dest_table = owner_table // per_dev
    targets = jnp.arange(slots, dtype=jnp.int32)
    mine = lax.dynamic_index_in_dim(dest_table, device, 0, keepdims=False)
    hit = mine[None, :] == targets[:, None]
    arrive = dest_table == device
    picks = jnp.sum(jnp.where(hit, jnp.arange(blocks_here, dtype=jnp.int32)[None, :], 0), 1)
    got_keys = lax.all_to_all(
        jnp.take(cache_k, picks, axis=0, mode="clip"), "seq", split_axis=0, concat_axis=0, tiled=True
    )
    got_values = lax.all_to_all(
        jnp.take(cache_v, picks, axis=0, mode="clip"), "seq", split_axis=0, concat_axis=0, tiled=True
    )
    slot_req = jnp.where(jnp.any(arrive, 1), jnp.sum(jnp.where(arrive, owner_table, 0), 1), -1)
    key_req = jnp.repeat(slot_req, block_len)
    keys_all = got_keys.reshape(slots * block_len, -1)
    values_all = got_values.reshape(slots * block_len, -1)

    query_f = q_new.astype(jnp.float32)
    key_f = k_new.astype(jnp.float32)
    square_q, square_k = lax.psum(
        (jnp.sum(query_f * query_f, -1), jnp.sum(key_f * key_f, -1)), "mp"
    )
    first_all = jnp.arange(slots, dtype=jnp.int32) * per_dev
    req_all, pos_all = token_meta(
        new_count, prefix_blocks.reshape(slots, per_dev), first_all, block_len, tokens_here
    )
    query_req = lax.dynamic_index_in_dim(req_all, device, 0, keepdims=False)
    position = lax.dynamic_index_in_dim(pos_all, device, 0, keepdims=False)
    normed_q = query_f * lax.rsqrt(square_q / width_all + 1e-06)[:, None] * q_gain
    normed_k = key_f * lax.rsqrt(square_k / width_all + 1e-06)[:, None] * k_gain
    queries = rotate(normed_q.reshape(tokens_here, heads_here, HD), position).astype(jnp.bfloat16)
    keys_here = rotate(normed_k.reshape(tokens_here, heads_here, HD), position).astype(jnp.bfloat16)
    order = jnp.arange(tokens_here, dtype=jnp.int32)
    causal = (query_req[:, None] == query_req[None, :]) & (order[:, None] >= order[None, :])
    seen = query_req[:, None] == key_req[None, :]

    heads = []
    for head in range(heads_here):
        cols = slice(head * HD, (head + 1) * HD)
        query_h = queries[:, head]
        best_n, total_n, weights_n = head_partial(query_h, keys_here[:, head], None, causal)
        best_c, total_c, weights_c = head_partial(query_h, keys_all[:, cols], None, seen)
        best = jnp.maximum(best_n, best_c)
        factor_n = jnp.exp(best_n - best)
        factor_c = jnp.exp(best_c - best)
        total = total_n * factor_n + total_c * factor_c
        accum = jnp.einsum(
            "tk,kd->td", weights_n, v_new[:, cols], preferred_element_type=jnp.float32
        ) * factor_n[:, None] + jnp.einsum(
            "tk,kd->td", weights_c, values_all[:, cols], preferred_element_type=jnp.float32
        ) * factor_c[:, None]
        heads.append((accum / total[:, None]).astype(jnp.bfloat16))
    return jnp.concatenate(heads, -1)


def solution(mesh):
    return jax.shard_map(
        shards,
        mesh=mesh,
        in_specs=(
            P("seq", "mp"),
            P("seq", "mp"),
            P("seq", "mp"),
            P("mp"),
            P("mp"),
            P("seq", None, "mp"),
            P("seq", None, "mp"),
            P(),
            P(),
            P(),
        ),
        out_specs=P("seq", "mp"),
        check_vma=False,
    )
```

```python
import jax
import jax.numpy as jnp
from jax import lax
from jax.sharding import PartitionSpec as P

HD = 128


NEGATIVE = -1e30


def rotate(field, position):
    half = field.shape[-1] // 2
    freq = 500000.0 ** (-(jnp.arange(half, dtype=jnp.float32) / half))
    angle = position.astype(jnp.float32)[:, None] * freq[None, :]
    cosine = jnp.cos(angle)[:, None, :]
    sine = jnp.sin(angle)[:, None, :]
    first = field[..., :half]
    second = field[..., half:]
    return jnp.concatenate([first * cosine - second * sine, second * cosine + first * sine], -1)


def token_meta(counts, prefix, first_req, block_len, tokens_here):
    cumul = jnp.cumsum(counts, axis=1)
    starts = cumul - counts
    order = jnp.arange(tokens_here, dtype=jnp.int32)
    local = jnp.sum((order[None, :, None] >= cumul[:, None, :]).astype(jnp.int32), -1)
    picker = (
        local[:, :, None] == jnp.arange(counts.shape[1], dtype=jnp.int32)[None, None, :]
    ).astype(jnp.int32)
    offset = order[None, :] - jnp.sum(picker * starts[:, None, :], -1)
    before = jnp.sum(picker * prefix[:, None, :], -1)
    return (first_req[:, None] + local, before * block_len + offset)


def head_partial(queries, keys_in, values_in, allowed):
    scores = jnp.einsum(
        "td,kd->tk", queries, keys_in, preferred_element_type=jnp.float32
    ) * queries.shape[-1] ** (-0.5)
    scores = jnp.where(allowed, scores, NEGATIVE)
    best = jnp.max(scores, -1)
    weights = jnp.where(allowed, jnp.exp(scores - best[:, None]), 0.0)
    total = jnp.sum(weights, -1)
    return best, total, weights.astype(jnp.bfloat16)


def mp_sum(x):
    size = lax.axis_size("mp")
    if size & (size - 1):
        return lax.psum(x, "mp")
    step = 1
    while step < size:
        x = x + lax.ppermute(x, "mp", [(i, i ^ step) for i in range(size)])
        step *= 2
    return x


def shards(
    q_new, k_new, v_new, q_gain, k_gain, cache_k, cache_v, new_count, prefix_blocks, block_req
):
    tokens_here = q_new.shape[0]
    width_all = q_new.shape[1] * lax.axis_size("mp")
    heads_here = q_new.shape[1] // HD
    block_len = cache_k.shape[1]
    blocks_here = cache_k.shape[0]
    slots = lax.axis_size("seq")
    device = lax.axis_index("seq")
    per_dev = new_count.shape[1]

    owner_table = block_req.reshape(slots, blocks_here)
    dest_table = owner_table // per_dev
    targets = jnp.arange(slots, dtype=jnp.int32)
    mine = lax.dynamic_index_in_dim(dest_table, device, 0, keepdims=False)
    hit = mine[None, :] == targets[:, None]
    arrive = dest_table == device
    picks = jnp.sum(jnp.where(hit, jnp.arange(blocks_here, dtype=jnp.int32)[None, :], 0), 1)
    got_keys = lax.all_to_all(
        jnp.take(cache_k, picks, axis=0, mode="clip"), "seq", split_axis=0, concat_axis=0, tiled=True
    )
    got_values = lax.all_to_all(
        jnp.take(cache_v, picks, axis=0, mode="clip"), "seq", split_axis=0, concat_axis=0, tiled=True
    )
    slot_req = jnp.where(jnp.any(arrive, 1), jnp.sum(jnp.where(arrive, owner_table, 0), 1), -1)
    key_req = jnp.repeat(slot_req, block_len)
    keys_all = got_keys.reshape(slots * block_len, -1)
    values_all = got_values.reshape(slots * block_len, -1)

    query_f = q_new.astype(jnp.float32)
    key_f = k_new.astype(jnp.float32)
    square_q, square_k = mp_sum(
        jnp.stack([jnp.sum(query_f * query_f, -1), jnp.sum(key_f * key_f, -1)])
    )
    first_all = jnp.arange(slots, dtype=jnp.int32) * per_dev
    req_all, pos_all = token_meta(
        new_count, prefix_blocks.reshape(slots, per_dev), first_all, block_len, tokens_here
    )
    query_req = lax.dynamic_index_in_dim(req_all, device, 0, keepdims=False)
    position = lax.dynamic_index_in_dim(pos_all, device, 0, keepdims=False)
    normed_q = query_f * lax.rsqrt(square_q / width_all + 1e-06)[:, None] * q_gain
    normed_k = key_f * lax.rsqrt(square_k / width_all + 1e-06)[:, None] * k_gain
    queries = rotate(normed_q.reshape(tokens_here, heads_here, HD), position).astype(jnp.bfloat16)
    keys_here = rotate(normed_k.reshape(tokens_here, heads_here, HD), position).astype(jnp.bfloat16)
    order = jnp.arange(tokens_here, dtype=jnp.int32)
    causal = (query_req[:, None] == query_req[None, :]) & (order[:, None] >= order[None, :])
    seen = query_req[:, None] == key_req[None, :]

    heads = []
    for head in range(heads_here):
        cols = slice(head * HD, (head + 1) * HD)
        query_h = queries[:, head]
        best_n, total_n, weights_n = head_partial(query_h, keys_here[:, head], None, causal)
        best_c, total_c, weights_c = head_partial(query_h, keys_all[:, cols], None, seen)
        best = jnp.maximum(best_n, best_c)
        factor_n = jnp.exp(best_n - best)
        factor_c = jnp.exp(best_c - best)
        total = total_n * factor_n + total_c * factor_c
        accum = jnp.einsum(
            "tk,kd->td", weights_n, v_new[:, cols], preferred_element_type=jnp.float32
        ) * factor_n[:, None] + jnp.einsum(
            "tk,kd->td", weights_c, values_all[:, cols], preferred_element_type=jnp.float32
        ) * factor_c[:, None]
        heads.append((accum / total[:, None]).astype(jnp.bfloat16))
    return jnp.concatenate(heads, -1)


def solution(mesh):
    return jax.shard_map(
        shards,
        mesh=mesh,
        in_specs=(
            P("seq", "mp"),
            P("seq", "mp"),
            P("seq", "mp"),
            P("mp"),
            P("mp"),
            P("seq", None, "mp"),
            P("seq", None, "mp"),
            P(),
            P(),
            P(),
        ),
        out_specs=P("seq", "mp"),
        check_vma=False,
    )
```

```python
import jax
import jax.numpy as jnp
from jax import lax
from jax.sharding import PartitionSpec as P

HD = 128


NEGATIVE = -1e30


def rotate(field, position):
    half = field.shape[-1] // 2
    freq = 500000.0 ** (-(jnp.arange(half, dtype=jnp.float32) / half))
    angle = position.astype(jnp.float32)[:, None] * freq[None, :]
    cosine = jnp.cos(angle)[:, None, :]
    sine = jnp.sin(angle)[:, None, :]
    first = field[..., :half]
    second = field[..., half:]
    return jnp.concatenate([first * cosine - second * sine, second * cosine + first * sine], -1)


def token_meta(counts, prefix, first_req, block_len, tokens_here):
    cumul = jnp.cumsum(counts, axis=1)
    starts = cumul - counts
    order = jnp.arange(tokens_here, dtype=jnp.int32)
    local = jnp.sum((order[None, :, None] >= cumul[:, None, :]).astype(jnp.int32), -1)
    picker = (
        local[:, :, None] == jnp.arange(counts.shape[1], dtype=jnp.int32)[None, None, :]
    ).astype(jnp.int32)
    offset = order[None, :] - jnp.sum(picker * starts[:, None, :], -1)
    before = jnp.sum(picker * prefix[:, None, :], -1)
    return (first_req[:, None] + local, before * block_len + offset)


def head_partial(queries, keys_in, values_in, allowed):
    scores = jnp.einsum(
        "td,kd->tk", queries, keys_in, preferred_element_type=jnp.float32
    ) * queries.shape[-1] ** (-0.5)
    scores = jnp.where(allowed, scores, NEGATIVE)
    best = jnp.max(scores, -1)
    weights = jnp.where(allowed, jnp.exp(scores - best[:, None]), 0.0)
    total = jnp.sum(weights, -1)
    return best, total, weights.astype(jnp.bfloat16)


def shards(
    q_new, k_new, v_new, q_gain, k_gain, cache_k, cache_v, new_count, prefix_blocks, block_req
):
    tokens_here = q_new.shape[0]
    width_all = q_new.shape[1] * lax.axis_size("mp")
    heads_here = q_new.shape[1] // HD
    block_len = cache_k.shape[1]
    blocks_here = cache_k.shape[0]
    slots = lax.axis_size("seq")
    device = lax.axis_index("seq")
    per_dev = new_count.shape[1]

    owner_table = block_req.reshape(slots, blocks_here)
    dest_table = owner_table // per_dev
    targets = jnp.arange(slots, dtype=jnp.int32)
    mine = lax.dynamic_index_in_dim(dest_table, device, 0, keepdims=False)
    hit = mine[None, :] == targets[:, None]
    arrive = dest_table == device
    picks = jnp.sum(jnp.where(hit, jnp.arange(blocks_here, dtype=jnp.int32)[None, :], 0), 1)
    got_keys = lax.all_to_all(
        jnp.take(cache_k, picks, axis=0, mode="clip"), "seq", split_axis=0, concat_axis=0, tiled=True
    )
    send_values = jnp.take(cache_v, picks, axis=0, mode="clip")
    split = (heads_here - 1) * HD
    got_values = [
        lax.all_to_all(part, "seq", split_axis=0, concat_axis=0, tiled=True)
        for part in (send_values[..., :split], send_values[..., split:])
    ]
    slot_req = jnp.where(jnp.any(arrive, 1), jnp.sum(jnp.where(arrive, owner_table, 0), 1), -1)
    key_req = jnp.repeat(slot_req, block_len)
    keys_all = got_keys.reshape(slots * block_len, -1)
    values_all = [part.reshape(slots * block_len, -1) for part in got_values]

    query_f = q_new.astype(jnp.float32)
    key_f = k_new.astype(jnp.float32)
    square_q, square_k = lax.psum(
        (jnp.sum(query_f * query_f, -1), jnp.sum(key_f * key_f, -1)), "mp"
    )
    first_all = jnp.arange(slots, dtype=jnp.int32) * per_dev
    req_all, pos_all = token_meta(
        new_count, prefix_blocks.reshape(slots, per_dev), first_all, block_len, tokens_here
    )
    query_req = lax.dynamic_index_in_dim(req_all, device, 0, keepdims=False)
    position = lax.dynamic_index_in_dim(pos_all, device, 0, keepdims=False)
    normed_q = query_f * lax.rsqrt(square_q / width_all + 1e-06)[:, None] * q_gain
    normed_k = key_f * lax.rsqrt(square_k / width_all + 1e-06)[:, None] * k_gain
    queries = rotate(normed_q.reshape(tokens_here, heads_here, HD), position).astype(jnp.bfloat16)
    keys_here = rotate(normed_k.reshape(tokens_here, heads_here, HD), position).astype(jnp.bfloat16)
    order = jnp.arange(tokens_here, dtype=jnp.int32)
    causal = (query_req[:, None] == query_req[None, :]) & (order[:, None] >= order[None, :])
    seen = query_req[:, None] == key_req[None, :]

    heads = []
    for head in range(heads_here):
        cols = slice(head * HD, (head + 1) * HD)
        query_h = queries[:, head]
        best_n, total_n, weights_n = head_partial(query_h, keys_here[:, head], None, causal)
        best_c, total_c, weights_c = head_partial(query_h, keys_all[:, cols], None, seen)
        best = jnp.maximum(best_n, best_c)
        factor_n = jnp.exp(best_n - best)
        factor_c = jnp.exp(best_c - best)
        total = total_n * factor_n + total_c * factor_c
        accum = jnp.einsum(
            "tk,kd->td", weights_n, v_new[:, cols], preferred_element_type=jnp.float32
        ) * factor_n[:, None] + jnp.einsum(
            "tk,kd->td",
            weights_c,
            values_all[0][:, cols] if head < heads_here - 1 else values_all[1],
            preferred_element_type=jnp.float32,
        ) * factor_c[:, None]
        heads.append((accum / total[:, None]).astype(jnp.bfloat16))
    return jnp.concatenate(heads, -1)


def solution(mesh):
    return jax.shard_map(
        shards,
        mesh=mesh,
        in_specs=(
            P("seq", "mp"),
            P("seq", "mp"),
            P("seq", "mp"),
            P("mp"),
            P("mp"),
            P("seq", None, "mp"),
            P("seq", None, "mp"),
            P(),
            P(),
            P(),
        ),
        out_specs=P("seq", "mp"),
        check_vma=False,
    )
```

```python
import jax
import jax.numpy as jnp
from jax import lax
from jax.sharding import PartitionSpec as P

HD = 128


NEGATIVE = -1e30


def rotate(field, position):
    half = field.shape[-1] // 2
    freq = 500000.0 ** (-(jnp.arange(half, dtype=jnp.float32) / half))
    angle = position.astype(jnp.float32)[:, None] * freq[None, :]
    cosine = jnp.cos(angle)[:, None, :]
    sine = jnp.sin(angle)[:, None, :]
    first = field[..., :half]
    second = field[..., half:]
    return jnp.concatenate([first * cosine - second * sine, second * cosine + first * sine], -1)


def token_meta(counts, prefix, first_req, block_len, tokens_here):
    cumul = jnp.cumsum(counts, axis=1)
    starts = cumul - counts
    order = jnp.arange(tokens_here, dtype=jnp.int32)
    local = jnp.sum((order[None, :, None] >= cumul[:, None, :]).astype(jnp.int32), -1)
    picker = (
        local[:, :, None] == jnp.arange(counts.shape[1], dtype=jnp.int32)[None, None, :]
    ).astype(jnp.int32)
    offset = order[None, :] - jnp.sum(picker * starts[:, None, :], -1)
    before = jnp.sum(picker * prefix[:, None, :], -1)
    return (first_req[:, None] + local, before * block_len + offset)


def head_partial(queries, keys_in, values_in, allowed):
    scores = jnp.einsum(
        "td,kd->tk", queries, keys_in, preferred_element_type=jnp.float32
    ) * queries.shape[-1] ** (-0.5)
    scores = jnp.where(allowed, scores, NEGATIVE)
    best = jnp.max(scores, -1)
    weights = jnp.where(allowed, jnp.exp(scores - best[:, None]), 0.0)
    total = jnp.sum(weights, -1)
    return lax.optimization_barrier((best, total, weights.astype(jnp.bfloat16)))


def shards(
    q_new, k_new, v_new, q_gain, k_gain, cache_k, cache_v, new_count, prefix_blocks, block_req
):
    tokens_here = q_new.shape[0]
    width_all = q_new.shape[1] * lax.axis_size("mp")
    heads_here = q_new.shape[1] // HD
    block_len = cache_k.shape[1]
    blocks_here = cache_k.shape[0]
    slots = lax.axis_size("seq")
    device = lax.axis_index("seq")
    per_dev = new_count.shape[1]

    owner_table = block_req.reshape(slots, blocks_here)
    dest_table = owner_table // per_dev
    targets = jnp.arange(slots, dtype=jnp.int32)
    mine = lax.dynamic_index_in_dim(dest_table, device, 0, keepdims=False)
    hit = mine[None, :] == targets[:, None]
    arrive = dest_table == device
    picks = jnp.sum(jnp.where(hit, jnp.arange(blocks_here, dtype=jnp.int32)[None, :], 0), 1)
    got_keys = lax.all_to_all(
        jnp.take(cache_k, picks, axis=0, mode="clip"), "seq", split_axis=0, concat_axis=0, tiled=True
    )
    got_values = lax.all_to_all(
        jnp.take(cache_v, picks, axis=0, mode="clip"), "seq", split_axis=0, concat_axis=0, tiled=True
    )
    slot_req = jnp.where(jnp.any(arrive, 1), jnp.sum(jnp.where(arrive, owner_table, 0), 1), -1)
    key_req = jnp.repeat(slot_req, block_len)
    keys_all = got_keys.reshape(slots * block_len, -1)
    values_all = got_values.reshape(slots * block_len, -1)

    query_f = q_new.astype(jnp.float32)
    key_f = k_new.astype(jnp.float32)
    square_q, square_k = lax.psum(
        (jnp.sum(query_f * query_f, -1), jnp.sum(key_f * key_f, -1)), "mp"
    )
    first_all = jnp.arange(slots, dtype=jnp.int32) * per_dev
    req_all, pos_all = token_meta(
        new_count, prefix_blocks.reshape(slots, per_dev), first_all, block_len, tokens_here
    )
    query_req = lax.dynamic_index_in_dim(req_all, device, 0, keepdims=False)
    position = lax.dynamic_index_in_dim(pos_all, device, 0, keepdims=False)
    normed_q = query_f * lax.rsqrt(square_q / width_all + 1e-06)[:, None] * q_gain
    normed_k = key_f * lax.rsqrt(square_k / width_all + 1e-06)[:, None] * k_gain
    queries = rotate(normed_q.reshape(tokens_here, heads_here, HD), position).astype(jnp.bfloat16)
    keys_here = rotate(normed_k.reshape(tokens_here, heads_here, HD), position).astype(jnp.bfloat16)
    order = jnp.arange(tokens_here, dtype=jnp.int32)
    causal = (query_req[:, None] == query_req[None, :]) & (order[:, None] >= order[None, :])
    seen = query_req[:, None] == key_req[None, :]

    heads = []
    for head in range(heads_here):
        cols = slice(head * HD, (head + 1) * HD)
        query_h = queries[:, head]
        best_n, total_n, weights_n = head_partial(query_h, keys_here[:, head], None, causal)
        best_c, total_c, weights_c = head_partial(query_h, keys_all[:, cols], None, seen)
        best = jnp.maximum(best_n, best_c)
        factor_n = jnp.exp(best_n - best)
        factor_c = jnp.exp(best_c - best)
        total = total_n * factor_n + total_c * factor_c
        accum = jnp.einsum(
            "tk,kd->td", weights_n, v_new[:, cols], preferred_element_type=jnp.float32
        ) * factor_n[:, None] + jnp.einsum(
            "tk,kd->td", weights_c, values_all[:, cols], preferred_element_type=jnp.float32
        ) * factor_c[:, None]
        heads.append((accum / total[:, None]).astype(jnp.bfloat16))
    return jnp.concatenate(heads, -1)


def solution(mesh):
    return jax.shard_map(
        shards,
        mesh=mesh,
        in_specs=(
            P("seq", "mp"),
            P("seq", "mp"),
            P("seq", "mp"),
            P("mp"),
            P("mp"),
            P("seq", None, "mp"),
            P("seq", None, "mp"),
            P(),
            P(),
            P(),
        ),
        out_specs=P("seq", "mp"),
        check_vma=False,
    )
```

```python
import jax
import jax.numpy as jnp
from jax import lax
from jax.sharding import PartitionSpec as P

HD = 128


NEGATIVE = -1e30


def rotate(field, position):
    half = field.shape[-1] // 2
    freq = 500000.0 ** (-(jnp.arange(half, dtype=jnp.float32) / half))
    angle = position.astype(jnp.float32)[:, None] * freq[None, :]
    cosine = jnp.cos(angle)[:, None, :]
    sine = jnp.sin(angle)[:, None, :]
    first = field[..., :half]
    second = field[..., half:]
    return jnp.concatenate([first * cosine - second * sine, second * cosine + first * sine], -1)


def token_meta(counts, prefix, first_req, block_len, tokens_here):
    cumul = jnp.cumsum(counts, axis=1)
    starts = cumul - counts
    order = jnp.arange(tokens_here, dtype=jnp.int32)
    local = jnp.sum((order[None, :, None] >= cumul[:, None, :]).astype(jnp.int32), -1)
    picker = (
        local[:, :, None] == jnp.arange(counts.shape[1], dtype=jnp.int32)[None, None, :]
    ).astype(jnp.int32)
    offset = order[None, :] - jnp.sum(picker * starts[:, None, :], -1)
    before = jnp.sum(picker * prefix[:, None, :], -1)
    return (first_req[:, None] + local, before * block_len + offset)


def head_partial(queries, keys_in, values_in, allowed):
    scores = jnp.einsum(
        "td,kd->tk", queries, keys_in, preferred_element_type=jnp.float32
    ) * queries.shape[-1] ** (-0.5)
    scores = jnp.where(allowed, scores, NEGATIVE)
    best = jnp.max(scores, -1)
    weights = jnp.where(allowed, jnp.exp(scores - best[:, None]), 0.0)
    total = jnp.sum(weights, -1)
    return lax.optimization_barrier((best, total, weights.astype(jnp.bfloat16)))


def shards(
    q_new, k_new, v_new, q_gain, k_gain, cache_k, cache_v, new_count, prefix_blocks, block_req
):
    tokens_here = q_new.shape[0]
    width_all = q_new.shape[1] * lax.axis_size("mp")
    heads_here = q_new.shape[1] // HD
    block_len = cache_k.shape[1]
    blocks_here = cache_k.shape[0]
    slots = lax.axis_size("seq")
    device = lax.axis_index("seq")
    per_dev = new_count.shape[1]

    owner_table = block_req.reshape(slots, blocks_here)
    dest_table = owner_table // per_dev
    targets = jnp.arange(slots, dtype=jnp.int32)
    mine = lax.dynamic_index_in_dim(dest_table, device, 0, keepdims=False)
    hit = mine[None, :] == targets[:, None]
    arrive = dest_table == device
    picks = jnp.sum(jnp.where(hit, jnp.arange(blocks_here, dtype=jnp.int32)[None, :], 0), 1)
    got_keys = lax.all_to_all(
        jnp.take(cache_k, picks, axis=0, mode="clip"), "seq", split_axis=0, concat_axis=0, tiled=True
    )
    got_values = lax.all_to_all(
        jnp.take(cache_v, picks, axis=0, mode="clip"), "seq", split_axis=0, concat_axis=0, tiled=True
    )
    slot_req = jnp.where(jnp.any(arrive, 1), jnp.sum(jnp.where(arrive, owner_table, 0), 1), -1)
    key_req = jnp.repeat(slot_req, block_len)
    keys_all = got_keys.reshape(slots * block_len, -1)
    values_all = got_values.reshape(slots * block_len, -1)

    query_f = q_new.astype(jnp.float32)
    key_f = k_new.astype(jnp.float32)
    square_q, square_k = lax.psum(
        (jnp.sum(query_f * query_f, -1), jnp.sum(key_f * key_f, -1)), "mp"
    )
    first_all = jnp.arange(slots, dtype=jnp.int32) * per_dev
    req_all, pos_all = token_meta(
        new_count, prefix_blocks.reshape(slots, per_dev), first_all, block_len, tokens_here
    )
    query_req = lax.dynamic_index_in_dim(req_all, device, 0, keepdims=False)
    position = lax.dynamic_index_in_dim(pos_all, device, 0, keepdims=False)
    normed_q = query_f * lax.rsqrt(square_q / width_all + 1e-06)[:, None] * q_gain
    normed_k = key_f * lax.rsqrt(square_k / width_all + 1e-06)[:, None] * k_gain
    queries = rotate(normed_q.reshape(tokens_here, heads_here, HD), position).astype(jnp.bfloat16)
    keys_here = rotate(normed_k.reshape(tokens_here, heads_here, HD), position).astype(jnp.bfloat16)
    order = jnp.arange(tokens_here, dtype=jnp.int32)
    causal = (query_req[:, None] == query_req[None, :]) & (order[:, None] >= order[None, :])
    seen = query_req[:, None] == key_req[None, :]

    heads = []
    for head in range(heads_here):
        cols = slice(head * HD, (head + 1) * HD)
        query_h = queries[:, head]
        best_n, total_n, weights_n = head_partial(query_h, keys_here[:, head], None, causal)
        best_c, total_c, weights_c = head_partial(query_h, keys_all[:, cols], None, seen)
        best = jnp.maximum(best_n, best_c)
        factor_n = jnp.exp(best_n - best)
        factor_c = jnp.exp(best_c - best)
        total = total_n * factor_n + total_c * factor_c
        accum_n, factor_c, total = lax.optimization_barrier(
            (
                jnp.einsum(
                    "tk,kd->td", weights_n, v_new[:, cols], preferred_element_type=jnp.float32
                )
                * factor_n[:, None],
                factor_c,
                total,
            )
        )
        accum = accum_n + jnp.einsum(
            "tk,kd->td", weights_c, values_all[:, cols], preferred_element_type=jnp.float32
        ) * factor_c[:, None]
        heads.append((accum / total[:, None]).astype(jnp.bfloat16))
    return jnp.concatenate(heads, -1)


def solution(mesh):
    return jax.shard_map(
        shards,
        mesh=mesh,
        in_specs=(
            P("seq", "mp"),
            P("seq", "mp"),
            P("seq", "mp"),
            P("mp"),
            P("mp"),
            P("seq", None, "mp"),
            P("seq", None, "mp"),
            P(),
            P(),
            P(),
        ),
        out_specs=P("seq", "mp"),
        check_vma=False,
    )
```

```python
import jax
import jax.numpy as jnp
from jax import lax
from jax.sharding import PartitionSpec as P

HD = 128


NEGATIVE = -1e30


def rotate(field, position):
    half = field.shape[-1] // 2
    freq = 500000.0 ** (-(jnp.arange(half, dtype=jnp.float32) / half))
    angle = position.astype(jnp.float32)[:, None] * freq[None, :]
    cosine = jnp.cos(angle)[:, None, :]
    sine = jnp.sin(angle)[:, None, :]
    first = field[..., :half]
    second = field[..., half:]
    return jnp.concatenate([first * cosine - second * sine, second * cosine + first * sine], -1)


def token_meta(counts, prefix, first_req, block_len, tokens_here):
    cumul = jnp.cumsum(counts, axis=1)
    starts = cumul - counts
    order = jnp.arange(tokens_here, dtype=jnp.int32)
    local = jnp.sum((order[None, :, None] >= cumul[:, None, :]).astype(jnp.int32), -1)
    picker = (
        local[:, :, None] == jnp.arange(counts.shape[1], dtype=jnp.int32)[None, None, :]
    ).astype(jnp.int32)
    offset = order[None, :] - jnp.sum(picker * starts[:, None, :], -1)
    before = jnp.sum(picker * prefix[:, None, :], -1)
    return (first_req[:, None] + local, before * block_len + offset)


def head_partial(queries, keys_in, values_in, allowed):
    scores = jnp.einsum(
        "td,kd->tk", queries, keys_in, preferred_element_type=jnp.float32
    ) * queries.shape[-1] ** (-0.5)
    scores = jnp.where(allowed, scores, NEGATIVE)
    best = jnp.max(scores, -1)
    weights = jnp.where(allowed, jnp.exp(scores - best[:, None]), 0.0)
    total = jnp.sum(weights, -1)
    return lax.optimization_barrier((best, total, weights.astype(jnp.bfloat16)))


def shards(
    q_new, k_new, v_new, q_gain, k_gain, cache_k, cache_v, new_count, prefix_blocks, block_req
):
    tokens_here = q_new.shape[0]
    width_all = q_new.shape[1] * lax.axis_size("mp")
    heads_here = q_new.shape[1] // HD
    block_len = cache_k.shape[1]
    blocks_here = cache_k.shape[0]
    slots = lax.axis_size("seq")
    device = lax.axis_index("seq")
    per_dev = new_count.shape[1]

    owner_table = block_req.reshape(slots, blocks_here)
    dest_table = owner_table // per_dev
    targets = jnp.arange(slots, dtype=jnp.int32)
    mine = lax.dynamic_index_in_dim(dest_table, device, 0, keepdims=False)
    hit = mine[None, :] == targets[:, None]
    arrive = dest_table == device
    picks = jnp.sum(jnp.where(hit, jnp.arange(blocks_here, dtype=jnp.int32)[None, :], 0), 1)
    got_keys = lax.all_to_all(
        jnp.take(cache_k, picks, axis=0, mode="clip"), "seq", split_axis=0, concat_axis=0, tiled=True
    )
    got_values = lax.all_to_all(
        jnp.take(cache_v, picks, axis=0, mode="clip"), "seq", split_axis=0, concat_axis=0, tiled=True
    )
    slot_req = jnp.where(jnp.any(arrive, 1), jnp.sum(jnp.where(arrive, owner_table, 0), 1), -1)
    key_req = jnp.repeat(slot_req, block_len)
    keys_all = got_keys.reshape(slots * block_len, -1)
    values_all = got_values.reshape(slots * block_len, -1)

    query_f = q_new.astype(jnp.float32)
    key_f = k_new.astype(jnp.float32)
    square_q, square_k = lax.psum(
        (jnp.sum(query_f * query_f, -1), jnp.sum(key_f * key_f, -1)), "mp"
    )
    first_all = jnp.arange(slots, dtype=jnp.int32) * per_dev
    req_all, pos_all = token_meta(
        new_count, prefix_blocks.reshape(slots, per_dev), first_all, block_len, tokens_here
    )
    query_req = lax.dynamic_index_in_dim(req_all, device, 0, keepdims=False)
    position = lax.dynamic_index_in_dim(pos_all, device, 0, keepdims=False)
    normed_q = query_f * lax.rsqrt(square_q / width_all + 1e-06)[:, None] * q_gain
    normed_k = key_f * lax.rsqrt(square_k / width_all + 1e-06)[:, None] * k_gain
    queries = rotate(normed_q.reshape(tokens_here, heads_here, HD), position).astype(jnp.bfloat16)
    keys_here = rotate(normed_k.reshape(tokens_here, heads_here, HD), position).astype(jnp.bfloat16)
    order = jnp.arange(tokens_here, dtype=jnp.int32)
    causal = (query_req[:, None] == query_req[None, :]) & (order[:, None] >= order[None, :])
    seen = query_req[:, None] == key_req[None, :]

    heads = []
    for head in range(heads_here):
        cols = slice(head * HD, (head + 1) * HD)
        query_h = queries[:, head]
        best_n, total_n, weights_n = head_partial(query_h, keys_here[:, head], None, causal)
        best_c, total_c, weights_c = head_partial(query_h, keys_all[:, cols], None, seen)
        best = jnp.maximum(best_n, best_c)
        factor_n = jnp.exp(best_n - best)
        factor_c = jnp.exp(best_c - best)
        total = total_n * factor_n + total_c * factor_c
        accum_n, factor_c, total = lax.optimization_barrier(
            (
                jnp.einsum(
                    "tk,kd->td", weights_n, v_new[:, cols], preferred_element_type=jnp.float32
                )
                * factor_n[:, None],
                factor_c,
                total,
            )
        )
        accum = accum_n + jnp.einsum(
            "tk,kd->td", weights_c, values_all[:, cols], preferred_element_type=jnp.float32
        ) * factor_c[:, None]
        heads.append((accum, jnp.broadcast_to(total[:, None], accum.shape)))
    accum = jnp.concatenate([part[0] for part in heads], -1)
    total = jnp.concatenate([part[1] for part in heads], -1)
    return (accum / total).astype(jnp.bfloat16)


def solution(mesh):
    return jax.shard_map(
        shards,
        mesh=mesh,
        in_specs=(
            P("seq", "mp"),
            P("seq", "mp"),
            P("seq", "mp"),
            P("mp"),
            P("mp"),
            P("seq", None, "mp"),
            P("seq", None, "mp"),
            P(),
            P(),
            P(),
        ),
        out_specs=P("seq", "mp"),
        check_vma=False,
    )
```
